512 devices in a mesh: adapter: 64 (over y, z), mp: 8 (over x, core).
Axes of the slice: x: 4, y: 4, z: 16, core: 2. Of those that a mesh axis runs over, the one named last changes fastest.
Arguments:
- tokens: bfloat16 [24576, 8192], P('adapter', 'mp'), may hold values from -6 to 6
- cotangent: bfloat16 [24576, 1024], P('adapter', 'mp'), may hold values from -6 to 6
- value_weight: bfloat16 [8192, 1024], P('mp', 'adapter'), may hold values from -0.0625 to 0.0625
- down_store: bfloat16 [128, 8, 1024, 64], P(None, 'mp', 'adapter'), may hold values from -0.0625 to 0.0625
- down_first: float32 [128, 8, 1024, 64], P(None, 'mp', 'adapter'), may hold values from -4 to 4
- down_second: float32 [128, 8, 1024, 64], P(None, 'mp', 'adapter'), may hold values from 0.01 to 1
- up_store: bfloat16 [128, 64, 1024], P(None, 'adapter', 'mp'), may hold values from -0.75 to 0.75
- up_first: float32 [128, 64, 1024], P(None, 'adapter', 'mp'), may hold values from -4 to 4
- up_second: float32 [128, 64, 1024], P(None, 'adapter', 'mp'), may hold values from 0.01 to 1
- tile_adapter: int32 [192], replicated, may hold values from 0 to 127
- tile_length: int32 [192], replicated, may hold values from 1 to 128, as said below
- adapter_slot: int32 [128], replicated, may hold values from 0 to 127, each once
Outputs:
- projected: bfloat16 [24576, 1024], P('adapter', 'mp')
- token_gradient: bfloat16 [24576, 8192], P('adapter', 'mp')
- new_down: float32 [128, 8, 1024, 64], P(None, 'mp', 'adapter')
- new_down_first: float32 [128, 8, 1024, 64], P(None, 'mp', 'adapter')
- new_down_second: float32 [128, 8, 1024, 64], P(None, 'mp', 'adapter')
- new_up: float32 [128, 64, 1024], P(None, 'adapter', 'mp')
- new_up_first: float32 [128, 64, 1024], P(None, 'adapter', 'mp')
- new_up_second: float32 [128, 64, 1024], P(None, 'adapter', 'mp')
The draws below stay inside these ranges and needn't reach their ends.
Inputs may be any that keep to these rules, and one draw needn't show every extreme that they name: `tile_length`: some tile is full in every draw. `adapter_slot`: each slot holds exactly one adapter.
All inputs are finite; a program needn't handle non-finite values.
Results may differ from the reference program's by a relative error of at most 0.0046.
Values may be sent and summed in bfloat16 or wider, within the bound.
No kernel may reach another device: no remote copies, remote signals or barrier semaphores. Data moves between devices by JAX's collectives and lax.ppermute only.
A program may use at most 64 MiB of HBM per device.

```python
import math
import jax
import jax.numpy as jnp
import numpy as np
from jax import lax

MODEL_WIDTH = 8192
VALUE_OUTPUTS = 1024
R = 64
TILE = 128
STEP = 100
ADAPTERS = 128
TOKEN_TOTAL = 24576
N_TILES = 192
N_MP = 8


def draw_tile_length(key, part):
    first_key, second_key = jax.random.split(jax.random.fold_in(key, 11))
    lengths = jax.random.randint(first_key, (N_TILES,), 1, TILE + 1)
    full_tile = jax.random.randint(second_key, (), 0, N_TILES)
    return jnp.where(jnp.arange(N_TILES) == full_tile, TILE, lengths).astype(jnp.int32)


def set_ends(array, rng, smallest, top_value):
    longest = array.shape.index(max(array.shape))
    spots = []
    for shift in (0, 1):
        where = [jax.random.randint(jax.random.fold_in(rng, axis), (), 0, length) for axis, length in enumerate(array.shape)]
        where[longest] = (where[longest] + shift) % array.shape[longest]
        spots.append(tuple(where))
    return array.at[spots[0]].set(smallest).at[spots[1]].set(top_value)


def shard_levels(key, shape, cuts, low, high):
    def one(dim, blocks):
        draws = jax.random.uniform(jax.random.fold_in(jax.random.fold_in(key, 6), dim), (blocks,), jnp.float32, low / len(cuts), high / len(cuts))
        return jnp.repeat(jnp.exp(draws), shape[dim] // blocks).reshape((-1,) + (1,) * (len(shape) - dim - 1))

    factor_of = one(*cuts[0])
    for cut in cuts[1:]:
        factor_of = factor_of * one(*cut)
    return factor_of


def rank_table(amount, lean):
    portions = [(1 << 20) // math.isqrt(standing ** lean) + 1 for standing in range(1, amount + 1)]
    deviation = 1 + sum(portions) // (1 << 30)
    return np.cumsum(np.array([max(1, weight // deviation) for weight in portions]))


def ranked(stream_key, shape, count, lean):
    table = rank_table(count, lean)
    lot = jax.random.randint(jax.random.fold_in(stream_key, 1), shape, 0, int(table[count - 1]))
    standing = jnp.searchsorted(jnp.asarray(table, jnp.int32), lot, side="right")
    return jax.random.permutation(jax.random.fold_in(stream_key, 2), count)[standing].astype(jnp.int32)


def scatter_about(stream_key, shape, spread, limit, cuts=(), kind=jnp.bfloat16):
    array = jax.random.normal(stream_key, shape, jnp.float32) * spread
    if len(cuts) > 0:
        array = shard_levels(stream_key, shape, cuts, -0.22, 0.18) * array
    return jnp.clip(array, min=-limit, max=limit).astype(kind)


def setup_inputs(seed: int = 0) -> dict:
    key_list = jax.random.split(jax.random.key(seed), 13)
    tokens = scatter_about(key_list[0], (TOKEN_TOTAL, MODEL_WIDTH), 1.0, 6.0, ((0, 64), (1, 8)))
    cotangent = scatter_about(key_list[1], (TOKEN_TOTAL, VALUE_OUTPUTS), 1.0, 6.0, ((0, 64), (1, 8)))
    value_weight = scatter_about(key_list[2], (MODEL_WIDTH, VALUE_OUTPUTS), MODEL_WIDTH ** -0.5, 0.0625, ((0, 8), (1, 64)))
    down_store = scatter_about(key_list[3], (ADAPTERS, N_MP, MODEL_WIDTH // N_MP, R), MODEL_WIDTH ** -0.5, 0.0625, ((1, 8), (2, 64)))
    down_first = scatter_about(key_list[4], (ADAPTERS, N_MP, MODEL_WIDTH // N_MP, R), 0.3, 4.0, ((1, 8), (2, 64)), jnp.float32)
    down_second = jnp.clip(jnp.exp(math.log(1.0) - 4.6051702 * jax.random.uniform(key_list[5], (ADAPTERS, N_MP, MODEL_WIDTH // N_MP, R), jnp.float32) ** shard_levels(key_list[5], (ADAPTERS, N_MP, MODEL_WIDTH // N_MP, R), ((1, 8), (2, 64)), -0.2, 0.2)), 0.01, 1.0)
    up_store = scatter_about(key_list[6], (ADAPTERS, R, VALUE_OUTPUTS), R ** -0.5, 0.75, ((1, 64), (2, 8)))
    up_first = scatter_about(key_list[7], (ADAPTERS, R, VALUE_OUTPUTS), 0.3, 4.0, ((1, 64), (2, 8)), jnp.float32)
    up_second = jnp.clip(jnp.exp(math.log(1.0) - 4.6051702 * jax.random.uniform(key_list[8], (ADAPTERS, R, VALUE_OUTPUTS), jnp.float32) ** shard_levels(key_list[8], (ADAPTERS, R, VALUE_OUTPUTS), ((1, 64), (2, 8)), -0.2, 0.2)), 0.01, 1.0)
    tile_adapter = set_ends(ranked(key_list[9], (N_TILES,), ADAPTERS, 2), jax.random.fold_in(key_list[9], 3), 0, ADAPTERS - 1).astype(jnp.int32)
    tile_length = draw_tile_length(jax.random.fold_in(key_list[12], 71), 0)
    adapter_slot = jax.random.permutation(key_list[11], ADAPTERS).astype(jnp.int32)
    return dict(tokens=tokens, cotangent=cotangent, value_weight=value_weight, down_store=down_store, down_first=down_first, down_second=down_second, up_store=up_store, up_first=up_first, up_second=up_second, tile_adapter=tile_adapter, tile_length=tile_length, adapter_slot=adapter_slot)


adapter_scale = 2.0
learn_rate = 0.001
beta_one = 0.9
beta_two = 0.999
adam_eps = 1e-08

def adam_step(store, first, second, gradient):
    new_first = beta_one * first + (1.0 - beta_one) * gradient
    new_second = beta_two * second + (1.0 - beta_two) * gradient * gradient
    corr_one = 1.0 - beta_one ** STEP
    corr_two = 1.0 - beta_two ** STEP
    moved = store.astype(jnp.float32) - learn_rate * (new_first / corr_one) / (jnp.sqrt(new_second / corr_two) + adam_eps)
    return (moved, new_first, new_second)

def reference(tokens, cotangent, value_weight, down_store, down_first, down_second, up_store, up_first, up_second, tile_adapter, tile_length, adapter_slot):
    down_all = down_store.reshape(ADAPTERS, MODEL_WIDTH, R)
    tile_adapter_slot = adapter_slot[tile_adapter].astype(jnp.int32)
    position = jnp.arange(TILE)
    active_rows = (position[None, :] < tile_length[:, None]).reshape(TOKEN_TOTAL, 1)
    masked = cotangent * active_rows.astype(jnp.bfloat16)
    frozen_value = jnp.dot(tokens, value_weight, preferred_element_type=jnp.float32)
    frozen_backward = jnp.dot(masked, value_weight.T, preferred_element_type=jnp.float32)
    token_tiles = tokens.reshape(N_TILES, TILE, MODEL_WIDTH)
    tile_mask = masked.reshape(N_TILES, TILE, VALUE_OUTPUTS)

    def tile_values(carry, item):
        down_gradient, up_gradient = carry
        tok_rows, row_mask, slot_index = item
        down_weight = down_all[slot_index]
        up_weight = up_store[slot_index]
        down_portion = jnp.dot(tok_rows, down_weight, preferred_element_type=jnp.float32).astype(jnp.bfloat16)
        adapter_term = jnp.dot(down_portion, up_weight, preferred_element_type=jnp.float32)
        backward_portion = (adapter_scale * jnp.dot(row_mask, up_weight.T, preferred_element_type=jnp.float32)).astype(jnp.bfloat16)
        adapter_backward = jnp.dot(backward_portion, down_weight.T, preferred_element_type=jnp.float32)
        tile_down = jnp.dot(tok_rows.T, backward_portion, preferred_element_type=jnp.float32)
        tile_up_weight = adapter_scale * jnp.dot(down_portion.T, row_mask, preferred_element_type=jnp.float32)
        down_gradient = down_gradient.at[slot_index].add(tile_down)
        up_gradient = up_gradient.at[slot_index].add(tile_up_weight)
        return ((down_gradient, up_gradient), (adapter_term, adapter_backward))
    initial_down = jnp.zeros((ADAPTERS, MODEL_WIDTH, R), jnp.float32)
    initial_up = jnp.zeros((ADAPTERS, R, VALUE_OUTPUTS), jnp.float32)
    (down_gradient, up_gradient), (adapter_terms, adapter_backwards) = lax.scan(tile_values, (initial_down, initial_up), (token_tiles, tile_mask, tile_adapter_slot))
    projected = ((frozen_value + adapter_scale * adapter_terms.reshape(TOKEN_TOTAL, VALUE_OUTPUTS)) * active_rows.astype(jnp.float32)).astype(jnp.bfloat16)
    token_gradient = (frozen_backward + adapter_backwards.reshape(TOKEN_TOTAL, MODEL_WIDTH)).astype(jnp.bfloat16)
    new_down, new_down_first, new_down_second = adam_step(down_store, down_first, down_second, down_gradient.reshape(down_store.shape))
    new_up, new_up_first, new_up_second = adam_step(up_store, up_first, up_second, up_gradient)
    return (projected, token_gradient, new_down, new_down_first, new_down_second, new_up, new_up_first, new_up_second)
```

```python
import jax
import jax.numpy as jnp
from jax import lax
from jax.sharding import Mesh, PartitionSpec as P

TILE = 128
STEP = 100


adapter_scale = 2.0
learn_rate = 0.001
beta_one = 0.9
beta_two = 0.999
adam_eps = 1e-08


def adam_step(store, first, second, gradient):
    new_first = beta_one * first + (1.0 - beta_one) * gradient
    new_second = beta_two * second + (1.0 - beta_two) * gradient * gradient
    corr_one = 1.0 - beta_one**STEP
    corr_two = 1.0 - beta_two**STEP
    moved = store.astype(jnp.float32) - learn_rate * (new_first / corr_one) / (
        jnp.sqrt(new_second / corr_two) + adam_eps
    )
    return (moved, new_first, new_second)


ADAPTER = ("ay", "az")


def gather_weight(value_weight):
    first = lax.all_gather(value_weight, "az", axis=1, tiled=True)
    return lax.all_gather(first, "ay", axis=1, tiled=True)


def split_adapter(mesh):
    devices = mesh.devices
    n_adapter = devices.shape[0]
    try:
        n_y = len({d.coords[1] for d in devices[:, 0]})
    except (AttributeError, IndexError, TypeError):
        n_y = 1
    if n_y < 1 or n_adapter % n_y:
        n_y = 1
    return Mesh(devices.reshape(n_y, n_adapter // n_y, devices.shape[1]), ("ay", "az", "mp"))


def shards(
    tokens,
    cotangent,
    value_weight,
    down_store,
    down_first,
    down_second,
    up_store,
    up_first,
    up_second,
    tile_adapter,
    tile_length,
    adapter_slot,
):
    tile_total = tile_adapter.shape[0]
    tok_count, feat_part = tokens.shape
    head_cols = cotangent.shape[1]
    tiles_here = tok_count // TILE
    adapter_count = adapter_slot.shape[0]
    my_index = lax.axis_index(ADAPTER)
    adapter_ids = jnp.arange(adapter_count, dtype=jnp.int32)
    tile_adapter_slot = jnp.sum(
        jnp.where(tile_adapter[:, None] == adapter_ids[None, :], adapter_slot[None, :], 0), axis=1
    )
    my_lengths = lax.dynamic_slice_in_dim(tile_length, my_index * tiles_here, tiles_here)
    active_rows = (jnp.arange(TILE)[None, :] < my_lengths[:, None]).reshape(tok_count, 1)
    masked_own = cotangent * active_rows.astype(jnp.bfloat16)
    masked_full = lax.all_gather(masked_own, "mp", axis=1, tiled=True)
    n_adapter = tile_total // tiles_here
    row_part = down_store.shape[2]
    rank = down_store.shape[3]
    sent_down = down_store[:, 0][tile_adapter_slot].reshape(tile_total, row_part * rank)
    sent_up = up_store[tile_adapter_slot].reshape(tile_total, head_cols)
    sent = jnp.concatenate([sent_down, sent_up], axis=1)
    arrived = lax.all_to_all(sent, ADAPTER, split_axis=0, concat_axis=0, tiled=True)
    arrived = arrived.reshape(n_adapter, tiles_here, row_part * rank + head_cols)
    down_panel = (
        arrived[:, :, : row_part * rank]
        .reshape(n_adapter, tiles_here, row_part, rank)
        .transpose(1, 0, 2, 3)
        .reshape(tiles_here, n_adapter * row_part, rank)
    )
    up_panel = arrived[:, :, row_part * rank :].transpose(1, 0, 2)
    w_full = gather_weight(value_weight)
    token_tiles = tokens.reshape(tiles_here, TILE, feat_part)
    frozen_part = jnp.dot(
        tokens,
        w_full,
        preferred_element_type=jnp.float32,
    )
    frozen_local = lax.psum_scatter(frozen_part, "mp", scatter_dimension=1, tiled=True)
    down_part = jnp.einsum(
        "ntd,ndr->ntr", token_tiles, down_panel, preferred_element_type=jnp.float32
    )
    down_sum = lax.psum(down_part, "mp")
    down_portion = down_sum.astype(jnp.bfloat16)
    adapter_term = jnp.einsum(
        "ntr,nrv->ntv", down_portion, up_panel, preferred_element_type=jnp.float32
    ).reshape(tok_count, head_cols)
    projected = (
        (frozen_local + adapter_scale * adapter_term) * active_rows.astype(jnp.float32)
    ).astype(jnp.bfloat16)
    tile_mask = masked_own.reshape(tiles_here, TILE, head_cols)
    backward_piece = adapter_scale * jnp.einsum(
        "ntv,nrv->ntr", tile_mask, up_panel, preferred_element_type=jnp.float32
    )
    backward_portion = lax.psum(backward_piece, "mp").astype(jnp.bfloat16)
    frozen_backward = lax.dot_general(
        masked_full,
        w_full,
        (((1,), (1,)), ((), ())),
        preferred_element_type=jnp.float32,
    )
    adapter_backward = jnp.einsum(
        "ntr,ndr->ntd", backward_portion, down_panel, preferred_element_type=jnp.float32
    ).reshape(tok_count, feat_part)
    token_gradient = (frozen_backward + adapter_backward).astype(jnp.bfloat16)
    home_down = jnp.einsum(
        "ntd,ntr->ndr", token_tiles, backward_portion, preferred_element_type=jnp.float32
    )
    local_up_weight = adapter_scale * jnp.einsum(
        "ntr,ntv->nrv", down_portion, tile_mask, preferred_element_type=jnp.float32
    )
    grads = jnp.concatenate(
        [home_down.reshape(tiles_here, n_adapter, row_part * rank), local_up_weight], axis=2
    )
    grads = lax.all_to_all(grads, ADAPTER, split_axis=1, concat_axis=0, tiled=True)
    arrived_down = grads[:, 0, : row_part * rank]
    arrived_up = grads[:, 0, row_part * rank :]
    selector = (adapter_ids[:, None] == tile_adapter_slot[None, :]).astype(jnp.float32)
    down_gradient = jnp.dot(
        selector, arrived_down.reshape(tile_total, -1), precision=lax.Precision.HIGHEST
    ).reshape(down_store.shape)
    up_gradient = jnp.dot(
        selector, arrived_up.reshape(tile_total, -1), precision=lax.Precision.HIGHEST
    ).reshape(up_store.shape)
    new_down, new_down_first, new_down_second = adam_step(
        down_store, down_first, down_second, down_gradient
    )
    new_up, new_up_first, new_up_second = adam_step(up_store, up_first, up_second, up_gradient)
    return (
        projected,
        token_gradient,
        new_down,
        new_down_first,
        new_down_second,
        new_up,
        new_up_first,
        new_up_second,
    )


def solution(mesh):
    mesh = split_adapter(mesh)
    placed = (
        P(ADAPTER, "mp"),
        P(ADAPTER, "mp"),
        P("mp", ADAPTER),
        P(None, "mp", ADAPTER, None),
        P(None, "mp", ADAPTER, None),
        P(None, "mp", ADAPTER, None),
        P(None, ADAPTER, "mp"),
        P(None, ADAPTER, "mp"),
        P(None, ADAPTER, "mp"),
        P(),
        P(),
        P(),
    )
    return jax.shard_map(
        shards,
        mesh=mesh,
        in_specs=placed,
        out_specs=(
            P(ADAPTER, "mp"),
            P(ADAPTER, "mp"),
            P(None, "mp", ADAPTER, None),
            P(None, "mp", ADAPTER, None),
            P(None, "mp", ADAPTER, None),
            P(None, ADAPTER, "mp"),
            P(None, ADAPTER, "mp"),
            P(None, ADAPTER, "mp"),
        ),
        check_vma=False,
    )
```

```python
import jax
import jax.numpy as jnp
from jax import lax
from jax.sharding import Mesh, PartitionSpec as P

TILE = 128
STEP = 100


adapter_scale = 2.0
learn_rate = 0.001
beta_one = 0.9
beta_two = 0.999
adam_eps = 1e-08


def adam_step(store, first, second, gradient):
    new_first = beta_one * first + (1.0 - beta_one) * gradient
    new_second = beta_two * second + (1.0 - beta_two) * gradient * gradient
    corr_one = 1.0 - beta_one**STEP
    corr_two = 1.0 - beta_two**STEP
    moved = store.astype(jnp.float32) - learn_rate * (new_first / corr_one) / (
        jnp.sqrt(new_second / corr_two) + adam_eps
    )
    return (moved, new_first, new_second)


ADAPTER = ("ay", "az")


def gather_weight(value_weight):
    n_z = lax.axis_size("az")
    rows, cols = value_weight.shape
    copies = jnp.broadcast_to(value_weight.T[None], (n_z, cols, rows))
    first = lax.all_to_all(copies, "az", split_axis=0, concat_axis=0, tiled=True)
    first = first.reshape(n_z * cols, rows).T
    return lax.all_gather(first, "ay", axis=1, tiled=True)


def split_adapter(mesh):
    devices = mesh.devices
    n_adapter = devices.shape[0]
    try:
        n_y = len({d.coords[1] for d in devices[:, 0]})
    except (AttributeError, IndexError, TypeError):
        n_y = 1
    if n_y < 1 or n_adapter % n_y:
        n_y = 1
    return Mesh(devices.reshape(n_y, n_adapter // n_y, devices.shape[1]), ("ay", "az", "mp"))


def shards(
    tokens,
    cotangent,
    value_weight,
    down_store,
    down_first,
    down_second,
    up_store,
    up_first,
    up_second,
    tile_adapter,
    tile_length,
    adapter_slot,
):
    tile_total = tile_adapter.shape[0]
    tok_count, feat_part = tokens.shape
    head_cols = cotangent.shape[1]
    tiles_here = tok_count // TILE
    adapter_count = adapter_slot.shape[0]
    my_index = lax.axis_index(ADAPTER)
    adapter_ids = jnp.arange(adapter_count, dtype=jnp.int32)
    tile_adapter_slot = jnp.sum(
        jnp.where(tile_adapter[:, None] == adapter_ids[None, :], adapter_slot[None, :], 0), axis=1
    )
    my_lengths = lax.dynamic_slice_in_dim(tile_length, my_index * tiles_here, tiles_here)
    active_rows = (jnp.arange(TILE)[None, :] < my_lengths[:, None]).reshape(tok_count, 1)
    masked_own = cotangent * active_rows.astype(jnp.bfloat16)
    masked_full = lax.all_gather(masked_own, "mp", axis=1, tiled=True)
    n_adapter = tile_total // tiles_here
    row_part = down_store.shape[2]
    rank = down_store.shape[3]
    sent_down = down_store[:, 0][tile_adapter_slot].reshape(tile_total, row_part * rank)
    sent_up = up_store[tile_adapter_slot].reshape(tile_total, head_cols)
    sent = jnp.concatenate([sent_down, sent_up], axis=1)
    arrived = lax.all_to_all(sent, ADAPTER, split_axis=0, concat_axis=0, tiled=True)
    arrived = arrived.reshape(n_adapter, tiles_here, row_part * rank + head_cols)
    down_panel = (
        arrived[:, :, : row_part * rank]
        .reshape(n_adapter, tiles_here, row_part, rank)
        .transpose(1, 0, 2, 3)
        .reshape(tiles_here, n_adapter * row_part, rank)
    )
    up_panel = arrived[:, :, row_part * rank :].transpose(1, 0, 2)
    w_full = gather_weight(value_weight)
    token_tiles = tokens.reshape(tiles_here, TILE, feat_part)
    frozen_part = jnp.dot(
        tokens,
        w_full,
        preferred_element_type=jnp.float32,
    )
    frozen_local = lax.psum_scatter(frozen_part, "mp", scatter_dimension=1, tiled=True)
    down_part = jnp.einsum(
        "ntd,ndr->ntr", token_tiles, down_panel, preferred_element_type=jnp.float32
    )
    down_sum = lax.psum(down_part, "mp")
    down_portion = down_sum.astype(jnp.bfloat16)
    adapter_term = jnp.einsum(
        "ntr,nrv->ntv", down_portion, up_panel, preferred_element_type=jnp.float32
    ).reshape(tok_count, head_cols)
    projected = (
        (frozen_local + adapter_scale * adapter_term) * active_rows.astype(jnp.float32)
    ).astype(jnp.bfloat16)
    tile_mask = masked_own.reshape(tiles_here, TILE, head_cols)
    backward_piece = adapter_scale * jnp.einsum(
        "ntv,nrv->ntr", tile_mask, up_panel, preferred_element_type=jnp.float32
    )
    backward_portion = lax.psum(backward_piece, "mp").astype(jnp.bfloat16)
    frozen_backward = lax.dot_general(
        masked_full,
        w_full,
        (((1,), (1,)), ((), ())),
        preferred_element_type=jnp.float32,
    )
    adapter_backward = jnp.einsum(
        "ntr,ndr->ntd", backward_portion, down_panel, preferred_element_type=jnp.float32
    ).reshape(tok_count, feat_part)
    token_gradient = (frozen_backward + adapter_backward).astype(jnp.bfloat16)
    home_down = jnp.einsum(
        "ntd,ntr->ndr", token_tiles, backward_portion, preferred_element_type=jnp.float32
    )
    local_up_weight = adapter_scale * jnp.einsum(
        "ntr,ntv->nrv", down_portion, tile_mask, preferred_element_type=jnp.float32
    )
    grads = jnp.concatenate(
        [home_down.reshape(tiles_here, n_adapter, row_part * rank), local_up_weight], axis=2
    )
    grads = lax.all_to_all(grads, ADAPTER, split_axis=1, concat_axis=0, tiled=True)
    arrived_down = grads[:, 0, : row_part * rank]
    arrived_up = grads[:, 0, row_part * rank :]
    selector = (adapter_ids[:, None] == tile_adapter_slot[None, :]).astype(jnp.float32)
    down_gradient = jnp.dot(
        selector, arrived_down.reshape(tile_total, -1), precision=lax.Precision.HIGHEST
    ).reshape(down_store.shape)
    up_gradient = jnp.dot(
        selector, arrived_up.reshape(tile_total, -1), precision=lax.Precision.HIGHEST
    ).reshape(up_store.shape)
    new_down, new_down_first, new_down_second = adam_step(
        down_store, down_first, down_second, down_gradient
    )
    new_up, new_up_first, new_up_second = adam_step(up_store, up_first, up_second, up_gradient)
    return (
        projected,
        token_gradient,
        new_down,
        new_down_first,
        new_down_second,
        new_up,
        new_up_first,
        new_up_second,
    )


def solution(mesh):
    mesh = split_adapter(mesh)
    placed = (
        P(ADAPTER, "mp"),
        P(ADAPTER, "mp"),
        P("mp", ADAPTER),
        P(None, "mp", ADAPTER, None),
        P(None, "mp", ADAPTER, None),
        P(None, "mp", ADAPTER, None),
        P(None, ADAPTER, "mp"),
        P(None, ADAPTER, "mp"),
        P(None, ADAPTER, "mp"),
        P(),
        P(),
        P(),
    )
    return jax.shard_map(
        shards,
        mesh=mesh,
        in_specs=placed,
        out_specs=(
            P(ADAPTER, "mp"),
            P(ADAPTER, "mp"),
            P(None, "mp", ADAPTER, None),
            P(None, "mp", ADAPTER, None),
            P(None, "mp", ADAPTER, None),
            P(None, ADAPTER, "mp"),
            P(None, ADAPTER, "mp"),
            P(None, ADAPTER, "mp"),
        ),
        check_vma=False,
    )
```

```python
import jax
import jax.numpy as jnp
from jax import lax
from jax.sharding import Mesh, PartitionSpec as P

TILE = 128
STEP = 100


adapter_scale = 2.0
learn_rate = 0.001
beta_one = 0.9
beta_two = 0.999
adam_eps = 1e-08


def adam_step(store, first, second, gradient):
    new_first = beta_one * first + (1.0 - beta_one) * gradient
    new_second = beta_two * second + (1.0 - beta_two) * gradient * gradient
    corr_one = 1.0 - beta_one**STEP
    corr_two = 1.0 - beta_two**STEP
    moved = store.astype(jnp.float32) - learn_rate * (new_first / corr_one) / (
        jnp.sqrt(new_second / corr_two) + adam_eps
    )
    return (moved, new_first, new_second)


ADAPTER = ("ay", "az")


def gather_along(piece, axis):
    count = lax.axis_size(axis)
    got = [piece]
    for shift in range(1, count):
        pairs = [(j, (j - shift) % count) for j in range(count)]
        got.append(lax.ppermute(piece, axis, pairs))
    ordered = jnp.roll(jnp.stack(got), lax.axis_index(axis), axis=0)
    return jnp.moveaxis(ordered, 0, 1).reshape(piece.shape[0], count * piece.shape[1])


def gather_weight(value_weight):
    return gather_along(gather_along(value_weight, "az"), "ay")


def split_adapter(mesh):
    devices = mesh.devices
    n_adapter = devices.shape[0]
    try:
        n_y = len({d.coords[1] for d in devices[:, 0]})
    except (AttributeError, IndexError, TypeError):
        n_y = 1
    if n_y < 1 or n_adapter % n_y:
        n_y = 1
    return Mesh(devices.reshape(n_y, n_adapter // n_y, devices.shape[1]), ("ay", "az", "mp"))


def shards(
    tokens,
    cotangent,
    value_weight,
    down_store,
    down_first,
    down_second,
    up_store,
    up_first,
    up_second,
    tile_adapter,
    tile_length,
    adapter_slot,
):
    tile_total = tile_adapter.shape[0]
    tok_count, feat_part = tokens.shape
    head_cols = cotangent.shape[1]
    tiles_here = tok_count // TILE
    adapter_count = adapter_slot.shape[0]
    my_index = lax.axis_index(ADAPTER)
    adapter_ids = jnp.arange(adapter_count, dtype=jnp.int32)
    tile_adapter_slot = jnp.sum(
        jnp.where(tile_adapter[:, None] == adapter_ids[None, :], adapter_slot[None, :], 0), axis=1
    )
    my_lengths = lax.dynamic_slice_in_dim(tile_length, my_index * tiles_here, tiles_here)
    active_rows = (jnp.arange(TILE)[None, :] < my_lengths[:, None]).reshape(tok_count, 1)
    masked_own = cotangent * active_rows.astype(jnp.bfloat16)
    masked_full = lax.all_gather(masked_own, "mp", axis=1, tiled=True)
    n_adapter = tile_total // tiles_here
    row_part = down_store.shape[2]
    rank = down_store.shape[3]
    sent_down = down_store[:, 0][tile_adapter_slot].reshape(tile_total, row_part * rank)
    sent_up = up_store[tile_adapter_slot].reshape(tile_total, head_cols)
    sent = jnp.concatenate([sent_down, sent_up], axis=1)
    arrived = lax.all_to_all(sent, ADAPTER, split_axis=0, concat_axis=0, tiled=True)
    arrived = arrived.reshape(n_adapter, tiles_here, row_part * rank + head_cols)
    down_panel = (
        arrived[:, :, : row_part * rank]
        .reshape(n_adapter, tiles_here, row_part, rank)
        .transpose(1, 0, 2, 3)
        .reshape(tiles_here, n_adapter * row_part, rank)
    )
    up_panel = arrived[:, :, row_part * rank :].transpose(1, 0, 2)
    w_full = gather_weight(value_weight)
    token_tiles = tokens.reshape(tiles_here, TILE, feat_part)
    frozen_part = jnp.dot(
        tokens,
        w_full,
        preferred_element_type=jnp.float32,
    )
    frozen_local = lax.psum_scatter(frozen_part, "mp", scatter_dimension=1, tiled=True)
    down_part = jnp.einsum(
        "ntd,ndr->ntr", token_tiles, down_panel, preferred_element_type=jnp.float32
    )
    down_sum = lax.psum(down_part, "mp")
    down_portion = down_sum.astype(jnp.bfloat16)
    adapter_term = jnp.einsum(
        "ntr,nrv->ntv", down_portion, up_panel, preferred_element_type=jnp.float32
    ).reshape(tok_count, head_cols)
    projected = (
        (frozen_local + adapter_scale * adapter_term) * active_rows.astype(jnp.float32)
    ).astype(jnp.bfloat16)
    tile_mask = masked_own.reshape(tiles_here, TILE, head_cols)
    backward_piece = adapter_scale * jnp.einsum(
        "ntv,nrv->ntr", tile_mask, up_panel, preferred_element_type=jnp.float32
    )
    backward_portion = lax.psum(backward_piece, "mp").astype(jnp.bfloat16)
    frozen_backward = lax.dot_general(
        masked_full,
        w_full,
        (((1,), (1,)), ((), ())),
        preferred_element_type=jnp.float32,
    )
    adapter_backward = jnp.einsum(
        "ntr,ndr->ntd", backward_portion, down_panel, preferred_element_type=jnp.float32
    ).reshape(tok_count, feat_part)
    token_gradient = (frozen_backward + adapter_backward).astype(jnp.bfloat16)
    home_down = jnp.einsum(
        "ntd,ntr->ndr", token_tiles, backward_portion, preferred_element_type=jnp.float32
    )
    local_up_weight = adapter_scale * jnp.einsum(
        "ntr,ntv->nrv", down_portion, tile_mask, preferred_element_type=jnp.float32
    )
    grads = jnp.concatenate(
        [home_down.reshape(tiles_here, n_adapter, row_part * rank), local_up_weight], axis=2
    )
    grads = lax.all_to_all(grads, ADAPTER, split_axis=1, concat_axis=0, tiled=True)
    arrived_down = grads[:, 0, : row_part * rank]
    arrived_up = grads[:, 0, row_part * rank :]
    selector = (adapter_ids[:, None] == tile_adapter_slot[None, :]).astype(jnp.float32)
    down_gradient = jnp.dot(
        selector, arrived_down.reshape(tile_total, -1), precision=lax.Precision.HIGHEST
    ).reshape(down_store.shape)
    up_gradient = jnp.dot(
        selector, arrived_up.reshape(tile_total, -1), precision=lax.Precision.HIGHEST
    ).reshape(up_store.shape)
    new_down, new_down_first, new_down_second = adam_step(
        down_store, down_first, down_second, down_gradient
    )
    new_up, new_up_first, new_up_second = adam_step(up_store, up_first, up_second, up_gradient)
    return (
        projected,
        token_gradient,
        new_down,
        new_down_first,
        new_down_second,
        new_up,
        new_up_first,
        new_up_second,
    )


def solution(mesh):
    mesh = split_adapter(mesh)
    placed = (
        P(ADAPTER, "mp"),
        P(ADAPTER, "mp"),
        P("mp", ADAPTER),
        P(None, "mp", ADAPTER, None),
        P(None, "mp", ADAPTER, None),
        P(None, "mp", ADAPTER, None),
        P(None, ADAPTER, "mp"),
        P(None, ADAPTER, "mp"),
        P(None, ADAPTER, "mp"),
        P(),
        P(),
        P(),
    )
    return jax.shard_map(
        shards,
        mesh=mesh,
        in_specs=placed,
        out_specs=(
            P(ADAPTER, "mp"),
            P(ADAPTER, "mp"),
            P(None, "mp", ADAPTER, None),
            P(None, "mp", ADAPTER, None),
            P(None, "mp", ADAPTER, None),
            P(None, ADAPTER, "mp"),
            P(None, ADAPTER, "mp"),
            P(None, ADAPTER, "mp"),
        ),
        check_vma=False,
    )
```

```python
import jax
import jax.numpy as jnp
from jax import lax
from jax.sharding import Mesh, PartitionSpec as P

TILE = 128
STEP = 100


adapter_scale = 2.0
learn_rate = 0.001
beta_one = 0.9
beta_two = 0.999
adam_eps = 1e-08


def adam_step(store, first, second, gradient):
    new_first = beta_one * first + (1.0 - beta_one) * gradient
    new_second = beta_two * second + (1.0 - beta_two) * gradient * gradient
    corr_one = 1.0 - beta_one**STEP
    corr_two = 1.0 - beta_two**STEP
    moved = store.astype(jnp.float32) - learn_rate * (new_first / corr_one) / (
        jnp.sqrt(new_second / corr_two) + adam_eps
    )
    return (moved, new_first, new_second)


ADAPTER = ("ay", "az")


def gather_weight(value_weight):
    rows, cols = value_weight.shape
    n_y = lax.axis_size("ay")
    n_z = lax.axis_size("az")
    first = lax.all_gather(value_weight, "ay", axis=1, tiled=True)
    whole = lax.all_gather(first, "az", axis=1, tiled=True)
    whole = whole.reshape(rows, n_z, n_y, cols).transpose(0, 2, 1, 3)
    return whole.reshape(rows, n_y * n_z * cols)


def split_adapter(mesh):
    devices = mesh.devices
    n_adapter = devices.shape[0]
    try:
        n_y = len({d.coords[1] for d in devices[:, 0]})
    except (AttributeError, IndexError, TypeError):
        n_y = 1
    if n_y < 1 or n_adapter % n_y:
        n_y = 1
    return Mesh(devices.reshape(n_y, n_adapter // n_y, devices.shape[1]), ("ay", "az", "mp"))


def shards(
    tokens,
    cotangent,
    value_weight,
    down_store,
    down_first,
    down_second,
    up_store,
    up_first,
    up_second,
    tile_adapter,
    tile_length,
    adapter_slot,
):
    tile_total = tile_adapter.shape[0]
    tok_count, feat_part = tokens.shape
    head_cols = cotangent.shape[1]
    tiles_here = tok_count // TILE
    adapter_count = adapter_slot.shape[0]
    my_index = lax.axis_index(ADAPTER)
    adapter_ids = jnp.arange(adapter_count, dtype=jnp.int32)
    tile_adapter_slot = jnp.sum(
        jnp.where(tile_adapter[:, None] == adapter_ids[None, :], adapter_slot[None, :], 0), axis=1
    )
    my_lengths = lax.dynamic_slice_in_dim(tile_length, my_index * tiles_here, tiles_here)
    active_rows = (jnp.arange(TILE)[None, :] < my_lengths[:, None]).reshape(tok_count, 1)
    masked_own = cotangent * active_rows.astype(jnp.bfloat16)
    masked_full = lax.all_gather(masked_own, "mp", axis=1, tiled=True)
    n_adapter = tile_total // tiles_here
    row_part = down_store.shape[2]
    rank = down_store.shape[3]
    sent_down = down_store[:, 0][tile_adapter_slot].reshape(tile_total, row_part * rank)
    sent_up = up_store[tile_adapter_slot].reshape(tile_total, head_cols)
    sent = jnp.concatenate([sent_down, sent_up], axis=1)
    arrived = lax.all_to_all(sent, ADAPTER, split_axis=0, concat_axis=0, tiled=True)
    arrived = arrived.reshape(n_adapter, tiles_here, row_part * rank + head_cols)
    down_panel = (
        arrived[:, :, : row_part * rank]
        .reshape(n_adapter, tiles_here, row_part, rank)
        .transpose(1, 0, 2, 3)
        .reshape(tiles_here, n_adapter * row_part, rank)
    )
    up_panel = arrived[:, :, row_part * rank :].transpose(1, 0, 2)
    w_full = gather_weight(value_weight)
    token_tiles = tokens.reshape(tiles_here, TILE, feat_part)
    frozen_part = jnp.dot(
        tokens,
        w_full,
        preferred_element_type=jnp.float32,
    )
    frozen_local = lax.psum_scatter(frozen_part, "mp", scatter_dimension=1, tiled=True)
    down_part = jnp.einsum(
        "ntd,ndr->ntr", token_tiles, down_panel, preferred_element_type=jnp.float32
    )
    down_sum = lax.psum(down_part, "mp")
    down_portion = down_sum.astype(jnp.bfloat16)
    adapter_term = jnp.einsum(
        "ntr,nrv->ntv", down_portion, up_panel, preferred_element_type=jnp.float32
    ).reshape(tok_count, head_cols)
    projected = (
        (frozen_local + adapter_scale * adapter_term) * active_rows.astype(jnp.float32)
    ).astype(jnp.bfloat16)
    tile_mask = masked_own.reshape(tiles_here, TILE, head_cols)
    backward_piece = adapter_scale * jnp.einsum(
        "ntv,nrv->ntr", tile_mask, up_panel, preferred_element_type=jnp.float32
    )
    backward_portion = lax.psum(backward_piece, "mp").astype(jnp.bfloat16)
    frozen_backward = lax.dot_general(
        masked_full,
        w_full,
        (((1,), (1,)), ((), ())),
        preferred_element_type=jnp.float32,
    )
    adapter_backward = jnp.einsum(
        "ntr,ndr->ntd", backward_portion, down_panel, preferred_element_type=jnp.float32
    ).reshape(tok_count, feat_part)
    token_gradient = (frozen_backward + adapter_backward).astype(jnp.bfloat16)
    home_down = jnp.einsum(
        "ntd,ntr->ndr", token_tiles, backward_portion, preferred_element_type=jnp.float32
    )
    local_up_weight = adapter_scale * jnp.einsum(
        "ntr,ntv->nrv", down_portion, tile_mask, preferred_element_type=jnp.float32
    )
    grads = jnp.concatenate(
        [home_down.reshape(tiles_here, n_adapter, row_part * rank), local_up_weight], axis=2
    )
    grads = lax.all_to_all(grads, ADAPTER, split_axis=1, concat_axis=0, tiled=True)
    arrived_down = grads[:, 0, : row_part * rank]
    arrived_up = grads[:, 0, row_part * rank :]
    selector = (adapter_ids[:, None] == tile_adapter_slot[None, :]).astype(jnp.float32)
    down_gradient = jnp.dot(
        selector, arrived_down.reshape(tile_total, -1), precision=lax.Precision.HIGHEST
    ).reshape(down_store.shape)
    up_gradient = jnp.dot(
        selector, arrived_up.reshape(tile_total, -1), precision=lax.Precision.HIGHEST
    ).reshape(up_store.shape)
    new_down, new_down_first, new_down_second = adam_step(
        down_store, down_first, down_second, down_gradient
    )
    new_up, new_up_first, new_up_second = adam_step(up_store, up_first, up_second, up_gradient)
    return (
        projected,
        token_gradient,
        new_down,
        new_down_first,
        new_down_second,
        new_up,
        new_up_first,
        new_up_second,
    )


def solution(mesh):
    mesh = split_adapter(mesh)
    placed = (
        P(ADAPTER, "mp"),
        P(ADAPTER, "mp"),
        P("mp", ADAPTER),
        P(None, "mp", ADAPTER, None),
        P(None, "mp", ADAPTER, None),
        P(None, "mp", ADAPTER, None),
        P(None, ADAPTER, "mp"),
        P(None, ADAPTER, "mp"),
        P(None, ADAPTER, "mp"),
        P(),
        P(),
        P(),
    )
    return jax.shard_map(
        shards,
        mesh=mesh,
        in_specs=placed,
        out_specs=(
            P(ADAPTER, "mp"),
            P(ADAPTER, "mp"),
            P(None, "mp", ADAPTER, None),
            P(None, "mp", ADAPTER, None),
            P(None, "mp", ADAPTER, None),
            P(None, ADAPTER, "mp"),
            P(None, ADAPTER, "mp"),
            P(None, ADAPTER, "mp"),
        ),
        check_vma=False,
    )
```

```python
import jax
import jax.numpy as jnp
from jax import lax
from jax.sharding import Mesh, PartitionSpec as P

TILE = 128
STEP = 100


adapter_scale = 2.0
learn_rate = 0.001
beta_one = 0.9
beta_two = 0.999
adam_eps = 1e-08


def adam_step(store, first, second, gradient):
    new_first = beta_one * first + (1.0 - beta_one) * gradient
    new_second = beta_two * second + (1.0 - beta_two) * gradient * gradient
    corr_one = 1.0 - beta_one**STEP
    corr_two = 1.0 - beta_two**STEP
    moved = store.astype(jnp.float32) - learn_rate * (new_first / corr_one) / (
        jnp.sqrt(new_second / corr_two) + adam_eps
    )
    return (moved, new_first, new_second)


ADAPTER = ("ay", "az")


def gather_weight(value_weight):
    rows, cols = value_weight.shape
    n_y = lax.axis_size("ay")
    n_z = lax.axis_size("az")
    first = lax.all_gather(value_weight, "ay", axis=1, tiled=True)
    whole = lax.all_gather(first, "az", axis=1, tiled=True)
    whole = whole.reshape(rows, n_z, n_y, cols).transpose(0, 2, 1, 3)
    return whole.reshape(rows, n_y * n_z * cols)


def exchange(x, axis):
    n_y = lax.axis_size("ay")
    n_z = lax.axis_size("az")
    shape = x.shape
    x = x.reshape(shape[:axis] + (n_y, n_z, shape[axis] // (n_y * n_z)) + shape[axis + 1 :])
    x = lax.all_to_all(x, "az", split_axis=axis + 1, concat_axis=axis + 1, tiled=True)
    x = lax.all_to_all(x, "ay", split_axis=axis, concat_axis=axis, tiled=True)
    return x.reshape(shape)


def split_adapter(mesh):
    devices = mesh.devices
    n_adapter = devices.shape[0]
    try:
        n_y = len({d.coords[1] for d in devices[:, 0]})
    except (AttributeError, IndexError, TypeError):
        n_y = 1
    if n_y < 1 or n_adapter % n_y:
        n_y = 1
    return Mesh(devices.reshape(n_y, n_adapter // n_y, devices.shape[1]), ("ay", "az", "mp"))


def shards(
    tokens,
    cotangent,
    value_weight,
    down_store,
    down_first,
    down_second,
    up_store,
    up_first,
    up_second,
    tile_adapter,
    tile_length,
    adapter_slot,
):
    tile_total = tile_adapter.shape[0]
    tok_count, feat_part = tokens.shape
    head_cols = cotangent.shape[1]
    tiles_here = tok_count // TILE
    adapter_count = adapter_slot.shape[0]
    my_index = lax.axis_index(ADAPTER)
    adapter_ids = jnp.arange(adapter_count, dtype=jnp.int32)
    tile_adapter_slot = jnp.sum(
        jnp.where(tile_adapter[:, None] == adapter_ids[None, :], adapter_slot[None, :], 0), axis=1
    )
    my_lengths = lax.dynamic_slice_in_dim(tile_length, my_index * tiles_here, tiles_here)
    active_rows = (jnp.arange(TILE)[None, :] < my_lengths[:, None]).reshape(tok_count, 1)
    masked_own = cotangent * active_rows.astype(jnp.bfloat16)
    masked_full = lax.all_gather(masked_own, "mp", axis=1, tiled=True)
    n_adapter = tile_total // tiles_here
    row_part = down_store.shape[2]
    rank = down_store.shape[3]
    sent_down = down_store[:, 0][tile_adapter_slot].reshape(tile_total, row_part * rank)
    sent_up = up_store[tile_adapter_slot].reshape(tile_total, head_cols)
    sent = jnp.concatenate([sent_down, sent_up], axis=1)
    arrived = exchange(sent, 0)
    arrived = arrived.reshape(n_adapter, tiles_here, row_part * rank + head_cols)
    down_panel = (
        arrived[:, :, : row_part * rank]
        .reshape(n_adapter, tiles_here, row_part, rank)
        .transpose(1, 0, 2, 3)
        .reshape(tiles_here, n_adapter * row_part, rank)
    )
    up_panel = arrived[:, :, row_part * rank :].transpose(1, 0, 2)
    w_full = gather_weight(value_weight)
    token_tiles = tokens.reshape(tiles_here, TILE, feat_part)
    frozen_part = jnp.dot(
        tokens,
        w_full,
        preferred_element_type=jnp.float32,
    )
    frozen_local = lax.psum_scatter(frozen_part, "mp", scatter_dimension=1, tiled=True)
    down_part = jnp.einsum(
        "ntd,ndr->ntr", token_tiles, down_panel, preferred_element_type=jnp.float32
    )
    down_sum = lax.psum(down_part, "mp")
    down_portion = down_sum.astype(jnp.bfloat16)
    adapter_term = jnp.einsum(
        "ntr,nrv->ntv", down_portion, up_panel, preferred_element_type=jnp.float32
    ).reshape(tok_count, head_cols)
    projected = (
        (frozen_local + adapter_scale * adapter_term) * active_rows.astype(jnp.float32)
    ).astype(jnp.bfloat16)
    tile_mask = masked_own.reshape(tiles_here, TILE, head_cols)
    backward_piece = adapter_scale * jnp.einsum(
        "ntv,nrv->ntr", tile_mask, up_panel, preferred_element_type=jnp.float32
    )
    backward_portion = lax.psum(backward_piece, "mp").astype(jnp.bfloat16)
    frozen_backward = lax.dot_general(
        masked_full,
        w_full,
        (((1,), (1,)), ((), ())),
        preferred_element_type=jnp.float32,
    )
    adapter_backward = jnp.einsum(
        "ntr,ndr->ntd", backward_portion, down_panel, preferred_element_type=jnp.float32
    ).reshape(tok_count, feat_part)
    token_gradient = (frozen_backward + adapter_backward).astype(jnp.bfloat16)
    home_down = jnp.einsum(
        "ntd,ntr->ndr", token_tiles, backward_portion, preferred_element_type=jnp.float32
    )
    local_up_weight = adapter_scale * jnp.einsum(
        "ntr,ntv->nrv", down_portion, tile_mask, preferred_element_type=jnp.float32
    )
    grads = jnp.concatenate(
        [home_down.reshape(tiles_here, n_adapter, row_part * rank), local_up_weight], axis=2
    )
    grads = exchange(grads, 1).transpose(1, 0, 2).reshape(tile_total, -1)
    arrived_down = grads[:, : row_part * rank]
    arrived_up = grads[:, row_part * rank :]
    selector = (adapter_ids[:, None] == tile_adapter_slot[None, :]).astype(jnp.float32)
    down_gradient = jnp.dot(
        selector, arrived_down.reshape(tile_total, -1), precision=lax.Precision.HIGHEST
    ).reshape(down_store.shape)
    up_gradient = jnp.dot(
        selector, arrived_up.reshape(tile_total, -1), precision=lax.Precision.HIGHEST
    ).reshape(up_store.shape)
    new_down, new_down_first, new_down_second = adam_step(
        down_store, down_first, down_second, down_gradient
    )
    new_up, new_up_first, new_up_second = adam_step(up_store, up_first, up_second, up_gradient)
    return (
        projected,
        token_gradient,
        new_down,
        new_down_first,
        new_down_second,
        new_up,
        new_up_first,
        new_up_second,
    )


def solution(mesh):
    mesh = split_adapter(mesh)
    placed = (
        P(ADAPTER, "mp"),
        P(ADAPTER, "mp"),
        P("mp", ADAPTER),
        P(None, "mp", ADAPTER, None),
        P(None, "mp", ADAPTER, None),
        P(None, "mp", ADAPTER, None),
        P(None, ADAPTER, "mp"),
        P(None, ADAPTER, "mp"),
        P(None, ADAPTER, "mp"),
        P(),
        P(),
        P(),
    )
    return jax.shard_map(
        shards,
        mesh=mesh,
        in_specs=placed,
        out_specs=(
            P(ADAPTER, "mp"),
            P(ADAPTER, "mp"),
            P(None, "mp", ADAPTER, None),
            P(None, "mp", ADAPTER, None),
            P(None, "mp", ADAPTER, None),
            P(None, ADAPTER, "mp"),
            P(None, ADAPTER, "mp"),
            P(None, ADAPTER, "mp"),
        ),
        check_vma=False,
    )
```

```python
import jax
import jax.numpy as jnp
from jax import lax
from jax.sharding import Mesh, PartitionSpec as P

TILE = 128
STEP = 100


adapter_scale = 2.0
learn_rate = 0.001
beta_one = 0.9
beta_two = 0.999
adam_eps = 1e-08


def adam_step(store, first, second, gradient):
    new_first = beta_one * first + (1.0 - beta_one) * gradient
    new_second = beta_two * second + (1.0 - beta_two) * gradient * gradient
    corr_one = 1.0 - beta_one**STEP
    corr_two = 1.0 - beta_two**STEP
    moved = store.astype(jnp.float32) - learn_rate * (new_first / corr_one) / (
        jnp.sqrt(new_second / corr_two) + adam_eps
    )
    return (moved, new_first, new_second)


ADAPTER = ("ay", "az")


def gather_weight(value_weight):
    rows, cols = value_weight.shape
    n_y = lax.axis_size("ay")
    n_z = lax.axis_size("az")
    first = lax.all_gather(value_weight, "ay", axis=1, tiled=True)
    whole = lax.all_gather(first, "az", axis=1, tiled=True)
    whole = whole.reshape(rows, n_z, n_y, cols).transpose(0, 2, 1, 3)
    return whole.reshape(rows, n_y * n_z * cols)


def exchange(x, axis):
    n_y = lax.axis_size("ay")
    n_z = lax.axis_size("az")
    shape = x.shape
    x = x.reshape(shape[:axis] + (n_y, n_z, shape[axis] // (n_y * n_z)) + shape[axis + 1 :])
    x = lax.all_to_all(x, "az", split_axis=axis + 1, concat_axis=axis + 1, tiled=True)
    x = lax.all_to_all(x, "ay", split_axis=axis, concat_axis=axis, tiled=True)
    return x.reshape(shape)


def split_adapter(mesh):
    devices = mesh.devices
    n_adapter = devices.shape[0]
    try:
        n_y = len({d.coords[1] for d in devices[:, 0]})
    except (AttributeError, IndexError, TypeError):
        n_y = 1
    if n_y < 1 or n_adapter % n_y:
        n_y = 1
    return Mesh(devices.reshape(n_y, n_adapter // n_y, devices.shape[1]), ("ay", "az", "mp"))


def shards(
    tokens,
    cotangent,
    value_weight,
    down_store,
    down_first,
    down_second,
    up_store,
    up_first,
    up_second,
    tile_adapter,
    tile_length,
    adapter_slot,
):
    tile_total = tile_adapter.shape[0]
    tok_count, feat_part = tokens.shape
    head_cols = cotangent.shape[1]
    tiles_here = tok_count // TILE
    adapter_count = adapter_slot.shape[0]
    my_index = lax.axis_index(ADAPTER)
    adapter_ids = jnp.arange(adapter_count, dtype=jnp.int32)
    tile_adapter_slot = jnp.sum(
        jnp.where(tile_adapter[:, None] == adapter_ids[None, :], adapter_slot[None, :], 0), axis=1
    )
    my_lengths = lax.dynamic_slice_in_dim(tile_length, my_index * tiles_here, tiles_here)
    active_rows = (jnp.arange(TILE)[None, :] < my_lengths[:, None]).reshape(tok_count, 1)
    masked_own = cotangent * active_rows.astype(jnp.bfloat16)
    masked_full = lax.all_gather(masked_own, "mp", axis=1, tiled=True)
    n_adapter = tile_total // tiles_here
    row_part = down_store.shape[2]
    rank = down_store.shape[3]
    sent_down = down_store[:, 0][tile_adapter_slot].reshape(tile_total, row_part * rank)
    sent_up = up_store[tile_adapter_slot].reshape(tile_total, head_cols)
    sent = jnp.concatenate([sent_down, sent_up], axis=1)
    arrived = exchange(sent, 0)
    arrived = arrived.reshape(n_adapter, tiles_here, row_part * rank + head_cols)
    down_panel = (
        arrived[:, :, : row_part * rank]
        .reshape(n_adapter, tiles_here, row_part, rank)
        .transpose(1, 0, 2, 3)
        .reshape(tiles_here, n_adapter * row_part, rank)
    )
    up_panel = arrived[:, :, row_part * rank :].transpose(1, 0, 2)
    w_full, masked_full = lax.optimization_barrier((gather_weight(value_weight), masked_full))
    token_tiles = tokens.reshape(tiles_here, TILE, feat_part)
    frozen_part = jnp.dot(
        tokens,
        w_full,
        preferred_element_type=jnp.float32,
    )
    frozen_local = lax.psum_scatter(frozen_part, "mp", scatter_dimension=1, tiled=True)
    down_part = jnp.einsum(
        "ntd,ndr->ntr", token_tiles, down_panel, preferred_element_type=jnp.float32
    )
    down_sum = lax.psum(down_part, "mp")
    down_portion = down_sum.astype(jnp.bfloat16)
    adapter_term = jnp.einsum(
        "ntr,nrv->ntv", down_portion, up_panel, preferred_element_type=jnp.float32
    ).reshape(tok_count, head_cols)
    projected = (
        (frozen_local + adapter_scale * adapter_term) * active_rows.astype(jnp.float32)
    ).astype(jnp.bfloat16)
    tile_mask = masked_own.reshape(tiles_here, TILE, head_cols)
    backward_piece = adapter_scale * jnp.einsum(
        "ntv,nrv->ntr", tile_mask, up_panel, preferred_element_type=jnp.float32
    )
    backward_portion = lax.psum(backward_piece, "mp").astype(jnp.bfloat16)
    frozen_backward = lax.dot_general(
        masked_full,
        w_full,
        (((1,), (1,)), ((), ())),
        preferred_element_type=jnp.float32,
    )
    adapter_backward = jnp.einsum(
        "ntr,ndr->ntd", backward_portion, down_panel, preferred_element_type=jnp.float32
    ).reshape(tok_count, feat_part)
    token_gradient = (frozen_backward + adapter_backward).astype(jnp.bfloat16)
    home_down = jnp.einsum(
        "ntd,ntr->ndr", token_tiles, backward_portion, preferred_element_type=jnp.float32
    )
    local_up_weight = adapter_scale * jnp.einsum(
        "ntr,ntv->nrv", down_portion, tile_mask, preferred_element_type=jnp.float32
    )
    grads = jnp.concatenate(
        [home_down.reshape(tiles_here, n_adapter, row_part * rank), local_up_weight], axis=2
    )
    grads = exchange(grads, 1).transpose(1, 0, 2).reshape(tile_total, -1)
    arrived_down = grads[:, : row_part * rank]
    arrived_up = grads[:, row_part * rank :]
    selector = (adapter_ids[:, None] == tile_adapter_slot[None, :]).astype(jnp.float32)
    down_gradient = jnp.dot(
        selector, arrived_down.reshape(tile_total, -1), precision=lax.Precision.HIGHEST
    ).reshape(down_store.shape)
    up_gradient = jnp.dot(
        selector, arrived_up.reshape(tile_total, -1), precision=lax.Precision.HIGHEST
    ).reshape(up_store.shape)
    new_down, new_down_first, new_down_second = adam_step(
        down_store, down_first, down_second, down_gradient
    )
    new_up, new_up_first, new_up_second = adam_step(up_store, up_first, up_second, up_gradient)
    return (
        projected,
        token_gradient,
        new_down,
        new_down_first,
        new_down_second,
        new_up,
        new_up_first,
        new_up_second,
    )


def solution(mesh):
    mesh = split_adapter(mesh)
    placed = (
        P(ADAPTER, "mp"),
        P(ADAPTER, "mp"),
        P("mp", ADAPTER),
        P(None, "mp", ADAPTER, None),
        P(None, "mp", ADAPTER, None),
        P(None, "mp", ADAPTER, None),
        P(None, ADAPTER, "mp"),
        P(None, ADAPTER, "mp"),
        P(None, ADAPTER, "mp"),
        P(),
        P(),
        P(),
    )
    return jax.shard_map(
        shards,
        mesh=mesh,
        in_specs=placed,
        out_specs=(
            P(ADAPTER, "mp"),
            P(ADAPTER, "mp"),
            P(None, "mp", ADAPTER, None),
            P(None, "mp", ADAPTER, None),
            P(None, "mp", ADAPTER, None),
            P(None, ADAPTER, "mp"),
            P(None, ADAPTER, "mp"),
            P(None, ADAPTER, "mp"),
        ),
        check_vma=False,
    )
```

```python
import jax
import jax.numpy as jnp
from jax import lax
from jax.sharding import Mesh, PartitionSpec as P

TILE = 128
STEP = 100


adapter_scale = 2.0
learn_rate = 0.001
beta_one = 0.9
beta_two = 0.999
adam_eps = 1e-08


def adam_step(store, first, second, gradient):
    new_first = beta_one * first + (1.0 - beta_one) * gradient
    new_second = beta_two * second + (1.0 - beta_two) * gradient * gradient
    corr_one = 1.0 - beta_one**STEP
    corr_two = 1.0 - beta_two**STEP
    moved = store.astype(jnp.float32) - learn_rate * (new_first / corr_one) / (
        jnp.sqrt(new_second / corr_two) + adam_eps
    )
    return (moved, new_first, new_second)


ADAPTER = ("ay", "az")
MP = ("mx", "mc")


def sum_over_mp(x):
    return lax.psum(lax.psum(x, "mc"), "mx")


def gather_weight(value_weight):
    rows, cols = value_weight.shape
    n_y = lax.axis_size("ay")
    n_z = lax.axis_size("az")
    first = lax.all_gather(value_weight, "ay", axis=1, tiled=True)
    whole = lax.all_gather(first, "az", axis=1, tiled=True)
    whole = whole.reshape(rows, n_z, n_y, cols).transpose(0, 2, 1, 3)
    return whole.reshape(rows, n_y * n_z * cols)


def exchange(x, axis):
    n_y = lax.axis_size("ay")
    n_z = lax.axis_size("az")
    shape = x.shape
    x = x.reshape(shape[:axis] + (n_y, n_z, shape[axis] // (n_y * n_z)) + shape[axis + 1 :])
    x = lax.all_to_all(x, "az", split_axis=axis + 1, concat_axis=axis + 1, tiled=True)
    x = lax.all_to_all(x, "ay", split_axis=axis, concat_axis=axis, tiled=True)
    return x.reshape(shape)


def split_adapter(mesh):
    devices = mesh.devices
    n_adapter = devices.shape[0]
    try:
        n_y = len({d.coords[1] for d in devices[:, 0]})
    except (AttributeError, IndexError, TypeError):
        n_y = 1
    if n_y < 1 or n_adapter % n_y:
        n_y = 1
    n_mp = devices.shape[1]
    try:
        n_c = len({d.core_on_chip for d in devices[0, :]})
    except (AttributeError, TypeError):
        n_c = 1
    if n_c < 1 or n_mp % n_c:
        n_c = 1
    shape = (n_y, n_adapter // n_y, n_mp // n_c, n_c)
    return Mesh(devices.reshape(shape), ("ay", "az", "mx", "mc"))


def shards(
    tokens,
    cotangent,
    value_weight,
    down_store,
    down_first,
    down_second,
    up_store,
    up_first,
    up_second,
    tile_adapter,
    tile_length,
    adapter_slot,
):
    tile_total = tile_adapter.shape[0]
    tok_count, feat_part = tokens.shape
    head_cols = cotangent.shape[1]
    tiles_here = tok_count // TILE
    adapter_count = adapter_slot.shape[0]
    my_index = lax.axis_index(ADAPTER)
    adapter_ids = jnp.arange(adapter_count, dtype=jnp.int32)
    tile_adapter_slot = jnp.sum(
        jnp.where(tile_adapter[:, None] == adapter_ids[None, :], adapter_slot[None, :], 0), axis=1
    )
    my_lengths = lax.dynamic_slice_in_dim(tile_length, my_index * tiles_here, tiles_here)
    active_rows = (jnp.arange(TILE)[None, :] < my_lengths[:, None]).reshape(tok_count, 1)
    masked_own = cotangent * active_rows.astype(jnp.bfloat16)
    masked_full = lax.all_gather(masked_own, MP, axis=1, tiled=True)
    n_adapter = tile_total // tiles_here
    row_part = down_store.shape[2]
    rank = down_store.shape[3]
    sent_down = down_store[:, 0][tile_adapter_slot].reshape(tile_total, row_part * rank)
    sent_up = up_store[tile_adapter_slot].reshape(tile_total, head_cols)
    sent = jnp.concatenate([sent_down, sent_up], axis=1)
    arrived = exchange(sent, 0)
    arrived = arrived.reshape(n_adapter, tiles_here, row_part * rank + head_cols)
    down_panel = (
        arrived[:, :, : row_part * rank]
        .reshape(n_adapter, tiles_here, row_part, rank)
        .transpose(1, 0, 2, 3)
        .reshape(tiles_here, n_adapter * row_part, rank)
    )
    up_panel = arrived[:, :, row_part * rank :].transpose(1, 0, 2)
    w_full, masked_full = lax.optimization_barrier((gather_weight(value_weight), masked_full))
    token_tiles = tokens.reshape(tiles_here, TILE, feat_part)
    frozen_part = jnp.dot(
        tokens,
        w_full,
        preferred_element_type=jnp.float32,
    )
    frozen_local = lax.psum_scatter(frozen_part, MP, scatter_dimension=1, tiled=True)
    down_part = jnp.einsum(
        "ntd,ndr->ntr", token_tiles, down_panel, preferred_element_type=jnp.float32
    )
    down_sum = sum_over_mp(down_part)
    down_portion = down_sum.astype(jnp.bfloat16)
    adapter_term = jnp.einsum(
        "ntr,nrv->ntv", down_portion, up_panel, preferred_element_type=jnp.float32
    ).reshape(tok_count, head_cols)
    projected = (
        (frozen_local + adapter_scale * adapter_term) * active_rows.astype(jnp.float32)
    ).astype(jnp.bfloat16)
    tile_mask = masked_own.reshape(tiles_here, TILE, head_cols)
    backward_piece = adapter_scale * jnp.einsum(
        "ntv,nrv->ntr", tile_mask, up_panel, preferred_element_type=jnp.float32
    )
    backward_portion = sum_over_mp(backward_piece).astype(jnp.bfloat16)
    frozen_backward = lax.dot_general(
        masked_full,
        w_full,
        (((1,), (1,)), ((), ())),
        preferred_element_type=jnp.float32,
    )
    adapter_backward = jnp.einsum(
        "ntr,ndr->ntd", backward_portion, down_panel, preferred_element_type=jnp.float32
    ).reshape(tok_count, feat_part)
    token_gradient = (frozen_backward + adapter_backward).astype(jnp.bfloat16)
    home_down = jnp.einsum(
        "ntd,ntr->ndr", token_tiles, backward_portion, preferred_element_type=jnp.float32
    )
    local_up_weight = adapter_scale * jnp.einsum(
        "ntr,ntv->nrv", down_portion, tile_mask, preferred_element_type=jnp.float32
    )
    grads = jnp.concatenate(
        [home_down.reshape(tiles_here, n_adapter, row_part * rank), local_up_weight], axis=2
    )
    grads = exchange(grads, 1).transpose(1, 0, 2).reshape(tile_total, -1)
    arrived_down = grads[:, : row_part * rank]
    arrived_up = grads[:, row_part * rank :]
    selector = (adapter_ids[:, None] == tile_adapter_slot[None, :]).astype(jnp.float32)
    down_gradient = jnp.dot(
        selector, arrived_down.reshape(tile_total, -1), precision=lax.Precision.HIGHEST
    ).reshape(down_store.shape)
    up_gradient = jnp.dot(
        selector, arrived_up.reshape(tile_total, -1), precision=lax.Precision.HIGHEST
    ).reshape(up_store.shape)
    new_down, new_down_first, new_down_second = adam_step(
        down_store, down_first, down_second, down_gradient
    )
    new_up, new_up_first, new_up_second = adam_step(up_store, up_first, up_second, up_gradient)
    return (
        projected,
        token_gradient,
        new_down,
        new_down_first,
        new_down_second,
        new_up,
        new_up_first,
        new_up_second,
    )


def solution(mesh):
    mesh = split_adapter(mesh)
    placed = (
        P(ADAPTER, MP),
        P(ADAPTER, MP),
        P(MP, ADAPTER),
        P(None, MP, ADAPTER, None),
        P(None, MP, ADAPTER, None),
        P(None, MP, ADAPTER, None),
        P(None, ADAPTER, MP),
        P(None, ADAPTER, MP),
        P(None, ADAPTER, MP),
        P(),
        P(),
        P(),
    )
    return jax.shard_map(
        shards,
        mesh=mesh,
        in_specs=placed,
        out_specs=(
            P(ADAPTER, MP),
            P(ADAPTER, MP),
            P(None, MP, ADAPTER, None),
            P(None, MP, ADAPTER, None),
            P(None, MP, ADAPTER, None),
            P(None, ADAPTER, MP),
            P(None, ADAPTER, MP),
            P(None, ADAPTER, MP),
        ),
        check_vma=False,
    )
```

```python
import jax
import jax.numpy as jnp
from jax import lax
from jax.sharding import Mesh, PartitionSpec as P

TILE = 128
STEP = 100


adapter_scale = 2.0
learn_rate = 0.001
beta_one = 0.9
beta_two = 0.999
adam_eps = 1e-08


def adam_step(store, first, second, gradient):
    new_first = beta_one * first + (1.0 - beta_one) * gradient
    new_second = beta_two * second + (1.0 - beta_two) * gradient * gradient
    corr_one = 1.0 - beta_one**STEP
    corr_two = 1.0 - beta_two**STEP
    moved = store.astype(jnp.float32) - learn_rate * (new_first / corr_one) / (
        jnp.sqrt(new_second / corr_two) + adam_eps
    )
    return (moved, new_first, new_second)


ADAPTER = ("ay", "az")


def gather_weight(value_weight):
    rows, cols = value_weight.shape
    n_y = lax.axis_size("ay")
    n_z = lax.axis_size("az")
    first = lax.all_gather(value_weight, "ay", axis=1, tiled=True)
    whole = lax.all_gather(first, "az", axis=1, tiled=True)
    whole = whole.reshape(rows, n_z, n_y, cols).transpose(0, 2, 1, 3)
    return whole.reshape(rows, n_y * n_z * cols)


def exchange(x, axis, y_first=False):
    n_y = lax.axis_size("ay")
    n_z = lax.axis_size("az")
    shape = x.shape
    x = x.reshape(shape[:axis] + (n_y, n_z, shape[axis] // (n_y * n_z)) + shape[axis + 1 :])
    if y_first:
        x = lax.all_to_all(x, "ay", split_axis=axis, concat_axis=axis, tiled=True)
    x = lax.all_to_all(x, "az", split_axis=axis + 1, concat_axis=axis + 1, tiled=True)
    if not y_first:
        x = lax.all_to_all(x, "ay", split_axis=axis, concat_axis=axis, tiled=True)
    return x.reshape(shape)


def split_adapter(mesh):
    devices = mesh.devices
    n_adapter = devices.shape[0]
    try:
        n_y = len({d.coords[1] for d in devices[:, 0]})
    except (AttributeError, IndexError, TypeError):
        n_y = 1
    if n_y < 1 or n_adapter % n_y:
        n_y = 1
    return Mesh(devices.reshape(n_y, n_adapter // n_y, devices.shape[1]), ("ay", "az", "mp"))


def shards(
    tokens,
    cotangent,
    value_weight,
    down_store,
    down_first,
    down_second,
    up_store,
    up_first,
    up_second,
    tile_adapter,
    tile_length,
    adapter_slot,
):
    tile_total = tile_adapter.shape[0]
    tok_count, feat_part = tokens.shape
    head_cols = cotangent.shape[1]
    tiles_here = tok_count // TILE
    adapter_count = adapter_slot.shape[0]
    my_index = lax.axis_index(ADAPTER)
    adapter_ids = jnp.arange(adapter_count, dtype=jnp.int32)
    tile_adapter_slot = jnp.sum(
        jnp.where(tile_adapter[:, None] == adapter_ids[None, :], adapter_slot[None, :], 0), axis=1
    )
    my_lengths = lax.dynamic_slice_in_dim(tile_length, my_index * tiles_here, tiles_here)
    active_rows = (jnp.arange(TILE)[None, :] < my_lengths[:, None]).reshape(tok_count, 1)
    masked_own = cotangent * active_rows.astype(jnp.bfloat16)
    masked_full = lax.all_gather(masked_own, "mp", axis=1, tiled=True)
    n_adapter = tile_total // tiles_here
    row_part = down_store.shape[2]
    rank = down_store.shape[3]
    sent_down = down_store[:, 0][tile_adapter_slot].reshape(tile_total, row_part * rank)
    sent_up = up_store[tile_adapter_slot].reshape(tile_total, head_cols)
    sent = jnp.concatenate([sent_down, sent_up], axis=1)
    arrived = exchange(sent, 0)
    arrived = arrived.reshape(n_adapter, tiles_here, row_part * rank + head_cols)
    down_panel = (
        arrived[:, :, : row_part * rank]
        .reshape(n_adapter, tiles_here, row_part, rank)
        .transpose(1, 0, 2, 3)
        .reshape(tiles_here, n_adapter * row_part, rank)
    )
    up_panel = arrived[:, :, row_part * rank :].transpose(1, 0, 2)
    w_full, masked_full = lax.optimization_barrier((gather_weight(value_weight), masked_full))
    token_tiles = tokens.reshape(tiles_here, TILE, feat_part)
    frozen_part = jnp.dot(
        tokens,
        w_full,
        preferred_element_type=jnp.float32,
    )
    frozen_local = lax.psum_scatter(frozen_part, "mp", scatter_dimension=1, tiled=True)
    down_part = jnp.einsum(
        "ntd,ndr->ntr", token_tiles, down_panel, preferred_element_type=jnp.float32
    )
    down_sum = lax.psum(down_part, "mp")
    down_portion = down_sum.astype(jnp.bfloat16)
    adapter_term = jnp.einsum(
        "ntr,nrv->ntv", down_portion, up_panel, preferred_element_type=jnp.float32
    ).reshape(tok_count, head_cols)
    projected = (
        (frozen_local + adapter_scale * adapter_term) * active_rows.astype(jnp.float32)
    ).astype(jnp.bfloat16)
    tile_mask = masked_own.reshape(tiles_here, TILE, head_cols)
    backward_piece = adapter_scale * jnp.einsum(
        "ntv,nrv->ntr", tile_mask, up_panel, preferred_element_type=jnp.float32
    )
    backward_portion = lax.psum(backward_piece, "mp").astype(jnp.bfloat16)
    frozen_backward = lax.dot_general(
        masked_full,
        w_full,
        (((1,), (1,)), ((), ())),
        preferred_element_type=jnp.float32,
    )
    adapter_backward = jnp.einsum(
        "ntr,ndr->ntd", backward_portion, down_panel, preferred_element_type=jnp.float32
    ).reshape(tok_count, feat_part)
    token_gradient = (frozen_backward + adapter_backward).astype(jnp.bfloat16)
    home_down = jnp.einsum(
        "ntd,ntr->ndr", token_tiles, backward_portion, preferred_element_type=jnp.float32
    )
    local_up_weight = adapter_scale * jnp.einsum(
        "ntr,ntv->nrv", down_portion, tile_mask, preferred_element_type=jnp.float32
    )
    grads = jnp.concatenate(
        [home_down.reshape(tiles_here, n_adapter, row_part * rank), local_up_weight], axis=2
    )
    grads = exchange(grads, 1, y_first=True).transpose(1, 0, 2).reshape(tile_total, -1)
    arrived_down = grads[:, : row_part * rank]
    arrived_up = grads[:, row_part * rank :]
    selector = (adapter_ids[:, None] == tile_adapter_slot[None, :]).astype(jnp.float32)
    down_gradient = jnp.dot(
        selector, arrived_down.reshape(tile_total, -1), precision=lax.Precision.HIGHEST
    ).reshape(down_store.shape)
    up_gradient = jnp.dot(
        selector, arrived_up.reshape(tile_total, -1), precision=lax.Precision.HIGHEST
    ).reshape(up_store.shape)
    new_down, new_down_first, new_down_second = adam_step(
        down_store, down_first, down_second, down_gradient
    )
    new_up, new_up_first, new_up_second = adam_step(up_store, up_first, up_second, up_gradient)
    return (
        projected,
        token_gradient,
        new_down,
        new_down_first,
        new_down_second,
        new_up,
        new_up_first,
        new_up_second,
    )


def solution(mesh):
    mesh = split_adapter(mesh)
    placed = (
        P(ADAPTER, "mp"),
        P(ADAPTER, "mp"),
        P("mp", ADAPTER),
        P(None, "mp", ADAPTER, None),
        P(None, "mp", ADAPTER, None),
        P(None, "mp", ADAPTER, None),
        P(None, ADAPTER, "mp"),
        P(None, ADAPTER, "mp"),
        P(None, ADAPTER, "mp"),
        P(),
        P(),
        P(),
    )
    return jax.shard_map(
        shards,
        mesh=mesh,
        in_specs=placed,
        out_specs=(
            P(ADAPTER, "mp"),
            P(ADAPTER, "mp"),
            P(None, "mp", ADAPTER, None),
            P(None, "mp", ADAPTER, None),
            P(None, "mp", ADAPTER, None),
            P(None, ADAPTER, "mp"),
            P(None, ADAPTER, "mp"),
            P(None, ADAPTER, "mp"),
        ),
        check_vma=False,
    )
```

```python
import jax
import jax.numpy as jnp
from jax import lax
from jax.sharding import Mesh, PartitionSpec as P

TILE = 128
STEP = 100


adapter_scale = 2.0
learn_rate = 0.001
beta_one = 0.9
beta_two = 0.999
adam_eps = 1e-08


def adam_step(store, first, second, gradient):
    new_first = beta_one * first + (1.0 - beta_one) * gradient
    new_second = beta_two * second + (1.0 - beta_two) * gradient * gradient
    corr_one = 1.0 - beta_one**STEP
    corr_two = 1.0 - beta_two**STEP
    moved = store.astype(jnp.float32) - learn_rate * (new_first / corr_one) / (
        jnp.sqrt(new_second / corr_two) + adam_eps
    )
    return (moved, new_first, new_second)


ADAPTER = ("ay", "az")


def gather_weight(first, cols):
    rows = first.shape[0]
    n_y = lax.axis_size("ay")
    n_z = lax.axis_size("az")
    whole = lax.all_gather(first, "az", axis=1, tiled=True)
    whole = whole.reshape(rows, n_z, n_y, cols).transpose(0, 2, 1, 3)
    return whole.reshape(rows, n_y * n_z * cols)


def exchange(x, axis):
    n_y = lax.axis_size("ay")
    n_z = lax.axis_size("az")
    shape = x.shape
    x = x.reshape(shape[:axis] + (n_y, n_z, shape[axis] // (n_y * n_z)) + shape[axis + 1 :])
    x = lax.all_to_all(x, "az", split_axis=axis + 1, concat_axis=axis + 1, tiled=True)
    x = lax.all_to_all(x, "ay", split_axis=axis, concat_axis=axis, tiled=True)
    return x.reshape(shape)


def split_adapter(mesh):
    devices = mesh.devices
    n_adapter = devices.shape[0]
    try:
        n_y = len({d.coords[1] for d in devices[:, 0]})
    except (AttributeError, IndexError, TypeError):
        n_y = 1
    if n_y < 1 or n_adapter % n_y:
        n_y = 1
    return Mesh(devices.reshape(n_y, n_adapter // n_y, devices.shape[1]), ("ay", "az", "mp"))


def shards(
    tokens,
    cotangent,
    value_weight,
    down_store,
    down_first,
    down_second,
    up_store,
    up_first,
    up_second,
    tile_adapter,
    tile_length,
    adapter_slot,
):
    tile_total = tile_adapter.shape[0]
    tok_count, feat_part = tokens.shape
    head_cols = cotangent.shape[1]
    tiles_here = tok_count // TILE
    adapter_count = adapter_slot.shape[0]
    my_index = lax.axis_index(ADAPTER)
    adapter_ids = jnp.arange(adapter_count, dtype=jnp.int32)
    tile_adapter_slot = jnp.sum(
        jnp.where(tile_adapter[:, None] == adapter_ids[None, :], adapter_slot[None, :], 0), axis=1
    )
    my_lengths = lax.dynamic_slice_in_dim(tile_length, my_index * tiles_here, tiles_here)
    active_rows = (jnp.arange(TILE)[None, :] < my_lengths[:, None]).reshape(tok_count, 1)
    masked_own = cotangent * active_rows.astype(jnp.bfloat16)
    masked_full = lax.all_gather(masked_own, "mp", axis=1, tiled=True)
    n_adapter = tile_total // tiles_here
    row_part = down_store.shape[2]
    rank = down_store.shape[3]
    sent_down = down_store[:, 0][tile_adapter_slot].reshape(tile_total, row_part * rank)
    sent_up = up_store[tile_adapter_slot].reshape(tile_total, head_cols)
    sent = jnp.concatenate([sent_down, sent_up], axis=1)
    w_first = lax.all_gather(value_weight, "ay", axis=1, tiled=True)
    w_first, sent = lax.optimization_barrier((w_first, sent))
    arrived = exchange(sent, 0)
    arrived = arrived.reshape(n_adapter, tiles_here, row_part * rank + head_cols)
    down_panel = (
        arrived[:, :, : row_part * rank]
        .reshape(n_adapter, tiles_here, row_part, rank)
        .transpose(1, 0, 2, 3)
        .reshape(tiles_here, n_adapter * row_part, rank)
    )
    up_panel = arrived[:, :, row_part * rank :].transpose(1, 0, 2)
    w_full, masked_full = lax.optimization_barrier((gather_weight(w_first, value_weight.shape[1]), masked_full))
    token_tiles = tokens.reshape(tiles_here, TILE, feat_part)
    frozen_part = jnp.dot(
        tokens,
        w_full,
        preferred_element_type=jnp.float32,
    )
    frozen_local = lax.psum_scatter(frozen_part, "mp", scatter_dimension=1, tiled=True)
    down_part = jnp.einsum(
        "ntd,ndr->ntr", token_tiles, down_panel, preferred_element_type=jnp.float32
    )
    down_sum = lax.psum(down_part, "mp")
    down_portion = down_sum.astype(jnp.bfloat16)
    adapter_term = jnp.einsum(
        "ntr,nrv->ntv", down_portion, up_panel, preferred_element_type=jnp.float32
    ).reshape(tok_count, head_cols)
    projected = (
        (frozen_local + adapter_scale * adapter_term) * active_rows.astype(jnp.float32)
    ).astype(jnp.bfloat16)
    tile_mask = masked_own.reshape(tiles_here, TILE, head_cols)
    backward_piece = adapter_scale * jnp.einsum(
        "ntv,nrv->ntr", tile_mask, up_panel, preferred_element_type=jnp.float32
    )
    backward_portion = lax.psum(backward_piece, "mp").astype(jnp.bfloat16)
    frozen_backward = lax.dot_general(
        masked_full,
        w_full,
        (((1,), (1,)), ((), ())),
        preferred_element_type=jnp.float32,
    )
    adapter_backward = jnp.einsum(
        "ntr,ndr->ntd", backward_portion, down_panel, preferred_element_type=jnp.float32
    ).reshape(tok_count, feat_part)
    token_gradient = (frozen_backward + adapter_backward).astype(jnp.bfloat16)
    home_down = jnp.einsum(
        "ntd,ntr->ndr", token_tiles, backward_portion, preferred_element_type=jnp.float32
    )
    local_up_weight = adapter_scale * jnp.einsum(
        "ntr,ntv->nrv", down_portion, tile_mask, preferred_element_type=jnp.float32
    )
    grads = jnp.concatenate(
        [home_down.reshape(tiles_here, n_adapter, row_part * rank), local_up_weight], axis=2
    )
    grads = exchange(grads, 1).transpose(1, 0, 2).reshape(tile_total, -1)
    arrived_down = grads[:, : row_part * rank]
    arrived_up = grads[:, row_part * rank :]
    selector = (adapter_ids[:, None] == tile_adapter_slot[None, :]).astype(jnp.float32)
    down_gradient = jnp.dot(
        selector, arrived_down.reshape(tile_total, -1), precision=lax.Precision.HIGHEST
    ).reshape(down_store.shape)
    up_gradient = jnp.dot(
        selector, arrived_up.reshape(tile_total, -1), precision=lax.Precision.HIGHEST
    ).reshape(up_store.shape)
    new_down, new_down_first, new_down_second = adam_step(
        down_store, down_first, down_second, down_gradient
    )
    new_up, new_up_first, new_up_second = adam_step(up_store, up_first, up_second, up_gradient)
    return (
        projected,
        token_gradient,
        new_down,
        new_down_first,
        new_down_second,
        new_up,
        new_up_first,
        new_up_second,
    )


def solution(mesh):
    mesh = split_adapter(mesh)
    placed = (
        P(ADAPTER, "mp"),
        P(ADAPTER, "mp"),
        P("mp", ADAPTER),
        P(None, "mp", ADAPTER, None),
        P(None, "mp", ADAPTER, None),
        P(None, "mp", ADAPTER, None),
        P(None, ADAPTER, "mp"),
        P(None, ADAPTER, "mp"),
        P(None, ADAPTER, "mp"),
        P(),
        P(),
        P(),
    )
    return jax.shard_map(
        shards,
        mesh=mesh,
        in_specs=placed,
        out_specs=(
            P(ADAPTER, "mp"),
            P(ADAPTER, "mp"),
            P(None, "mp", ADAPTER, None),
            P(None, "mp", ADAPTER, None),
            P(None, "mp", ADAPTER, None),
            P(None, ADAPTER, "mp"),
            P(None, ADAPTER, "mp"),
            P(None, ADAPTER, "mp"),
        ),
        check_vma=False,
    )
```
